256 devices in a mesh: ctx: 64 (over x_hi, z, y), head: 4 (over x_lo, core).
Axes of the slice: x: 4 (x_hi: 2, x_lo: 2; x = x_hi * 2 + x_lo), y: 4, z: 8, core: 2. Of those that a mesh axis runs over, the one named last changes fastest.
Arguments:
- queries: bfloat16 [8192, 16, 128], P('ctx', 'head'), may hold values from -30 to 30
- rotated_keys: bfloat16 [8192, 8, 128], P('ctx', 'head'), may hold values from -4 to 4
- value_vectors: bfloat16 [8192, 8, 128], P('ctx', 'head'), may hold values from -6 to 6
- out_grad: bfloat16 [8192, 5376], P('ctx', 'head'), may hold values from -16 to 16
- out_proj: bfloat16 [5376, 2048], P('ctx', 'head'), may hold values from -0.125 to 0.125
- seg_ids: int32 [8192], replicated, may hold values from 0 to 15, never falling along the last dimension, each value on 1 to 4096 neighbouring positions
Outputs:
- layer_out: bfloat16 [8192, 5376], P('ctx', 'head')
- query_gradient: bfloat16 [8192, 16, 128], P('ctx', 'head')
- grad_key: bfloat16 [8192, 8, 128], P('ctx', 'head')
- grad_value: bfloat16 [8192, 8, 128], P('ctx', 'head')
- grad_proj: float32 [5376, 2048], P('ctx', 'head')
The draws below stay inside these ranges and needn't reach their ends.
Inputs may be any that keep to these rules, and one draw needn't show every extreme that they name: `seg_ids`: segment ids never fall along the slab; every one of the 16 books holds one token or more.
All inputs are finite; a program needn't handle non-finite values.
Results may differ from the reference program's by a relative error of at most 0.025.
Values may be sent and summed in bfloat16 or wider, within the bound.
No kernel may reach another device: no remote copies, remote signals or barrier semaphores. Data moves between devices by JAX's collectives and lax.ppermute only.
A program may use at most 128 MiB of HBM per device.

```python
import math
import jax
import jax.numpy as jnp
import numpy as np
from jax import lax

D = 5376
HEAD_WIDTH = 128
WINDOW_TOKENS = 1024
HQ = 16
KEY_VALUE_HEADS = 8
SLAB_TOKENS = 8192
QUERIES_PER_KV = 2
SEGMENTS = 16


def drawn_pair(key):
    base_key = jax.random.fold_in(key, 4711)
    first_key, second_random_key = jax.random.split(base_key, 2)
    query_draw = jnp.clip(2.5 * jax.random.normal(first_key, (SLAB_TOKENS, HQ, HEAD_WIDTH), jnp.float32), -10.0, 10.0)
    random_key_draw = jnp.clip(jax.random.normal(second_random_key, (SLAB_TOKENS, KEY_VALUE_HEADS, HEAD_WIDTH), jnp.float32), -4.0, 4.0)
    return (query_draw, random_key_draw)


def draw_queries(key, part):
    return drawn_pair(key)[0].astype(jnp.bfloat16)


def draw_rotated_keys(key, part):
    return drawn_pair(key)[1].astype(jnp.bfloat16)


def with_spikes(result, own_key, source, target, parts, factor):
    owner, partner = [(jnp.arange(result.shape[position]) // (result.shape[position] // parts)).reshape([-1 if axis == position else 1 for axis in range(result.ndim)]) for position in (source, target)]
    chosen = jax.random.permutation(own_key, parts)[partner]
    strong = (owner == chosen) | (owner == (partner + parts // 2) % parts)
    return jnp.where(strong, factor * result, result)


def block_scale(rng, dims, cuts, low, top_value):
    level = 1.0
    for position, shards_of in cuts:
        steps = jax.random.uniform(jax.random.fold_in(jax.random.fold_in(rng, 6), position), (shards_of,), jnp.float32, low / len(cuts), top_value / len(cuts))
        level = level * jnp.repeat(jnp.exp(steps), dims[position] // shards_of).reshape((-1,) + (1,) * (len(dims) - 1 - position))
    return level


def profile(count, total, bound, skew):
    loads = [(1 << 20) // math.isqrt(grade ** skew) + 1 for grade in range(2, count + 1)]
    spare, counts = total - bound - (count - 1), [1] * (count - 1)
    while spare > 0:
        movable = [i for i in range(count - 1) if counts[i] < bound]
        mass, left = sum([loads[i] for i in movable]), spare
        for i in movable:
            more = min(bound - counts[i], max(1, left * loads[i] // mass), spare)
            counts[i] = counts[i] + more
            spare = spare - more
    return np.array([bound] + counts)


def uneven_parts(rng, amount, total, reach, skew):
    if amount == 2:
        one = jax.random.randint(rng, (), max(1, total - reach), min(reach, total - 1) + 1)
        return jnp.stack([one, total - one])
    lengths = jnp.asarray(profile(amount, total, reach, skew), jnp.int32)
    twos = (amount - 1) // 2
    source_of, taker = lengths[1:1 + 2 * twos:2], lengths[2:2 + 2 * twos:2]
    slack = jnp.minimum(source_of - 1, reach - taker)
    moved = jax.random.randint(jax.random.fold_in(rng, 1), (twos,), 0, 1 << 20) % (slack + 1)
    lengths = lengths.at[1:1 + 2 * twos:2].set(source_of - moved).at[2:2 + 2 * twos:2].set(taker + moved)
    return lengths[jax.random.permutation(jax.random.fold_in(rng, 2), amount)]


def normal_values(key, extent, scale, most, pieces=(), kind=jnp.bfloat16):
    values = jax.random.normal(key, extent, jnp.float32) * scale
    if len(pieces) > 0:
        values = block_scale(key, extent, pieces, -0.22, 0.18) * values
    return jnp.clip(values, min=-most, max=most).astype(kind)


def bell_draw_with(rng, shape, spread, reach, cuts, heavy, kind=jnp.bfloat16):
    result = spread * jax.random.normal(rng, shape, jnp.float32)
    if cuts:
        result = result * block_scale(rng, shape, cuts, -0.22, 0.18)
    return jnp.clip(with_spikes(result, jax.random.fold_in(rng, 3), *heavy), -reach, reach).astype(kind)


def setup_inputs(seed: int = 0) -> dict:
    seeds = jax.random.split(jax.random.key(seed), 7)
    return {
        "queries": draw_queries(jax.random.fold_in(seeds[6], 71), 0),
        "rotated_keys": draw_rotated_keys(jax.random.fold_in(seeds[6], 71), 0),
        "value_vectors": normal_values(seeds[2], (SLAB_TOKENS, KEY_VALUE_HEADS, HEAD_WIDTH), 1.0, 6.0, ((0, 64), (1, 4))),
        "out_grad": bell_draw_with(seeds[3], (SLAB_TOKENS, D), 1.0, 16.0, ((0, 64), (1, 4)), (0, 1, 64, 4.0)),
        "out_proj": normal_values(seeds[4], (D, HQ * HEAD_WIDTH), (HQ * HEAD_WIDTH) ** -0.5, 0.125, ((0, 64), (1, 4))),
        "seg_ids": jnp.searchsorted(jnp.cumsum(uneven_parts(seeds[5], SEGMENTS, SLAB_TOKENS, SLAB_TOKENS // 2, 2)), jnp.arange(SLAB_TOKENS), side="right").astype(jnp.int32),
    }


def reference(queries, rotated_keys, value_vectors, out_grad, out_proj, seg_ids):
    logit_scale = 168.0 ** -0.5
    rows_per_block = math.gcd(SLAB_TOKENS, 512)
    block_count = SLAB_TOKENS // rows_per_block
    span_rows = WINDOW_TOKENS + rows_per_block
    padded_keys = jnp.concatenate([jnp.zeros((WINDOW_TOKENS, KEY_VALUE_HEADS, HEAD_WIDTH), rotated_keys.dtype), rotated_keys], 0)
    padded_values = jnp.concatenate([jnp.zeros((WINDOW_TOKENS, KEY_VALUE_HEADS, HEAD_WIDTH), value_vectors.dtype), value_vectors], 0)
    seg_whole = seg_ids.astype(jnp.int32)
    seg_padded = jnp.concatenate([jnp.full((WINDOW_TOKENS,), -1, jnp.int32), seg_whole], 0)

    def block_probs(block_index):
        first_row = (block_index * rows_per_block).astype(jnp.int32)
        block_queries = lax.dynamic_slice_in_dim(queries, first_row, rows_per_block, 0).astype(jnp.float32)
        block_queries = block_queries.reshape(rows_per_block, KEY_VALUE_HEADS, QUERIES_PER_KV, HEAD_WIDTH)
        block_keys = lax.dynamic_slice_in_dim(padded_keys, first_row, span_rows, 0).astype(jnp.float32)
        block_values = lax.dynamic_slice_in_dim(padded_values, first_row, span_rows, 0).astype(jnp.float32)
        query_pos = first_row + jnp.arange(rows_per_block, dtype=jnp.int32)
        key_pos = first_row - WINDOW_TOKENS + jnp.arange(span_rows, dtype=jnp.int32)
        query_seg = lax.dynamic_slice_in_dim(seg_whole, first_row, rows_per_block, 0)
        key_seg = lax.dynamic_slice_in_dim(seg_padded, first_row, span_rows, 0)
        allowed = (key_pos[None, :] <= query_pos[:, None]) & (query_pos[:, None] - key_pos[None, :] < WINDOW_TOKENS)
        allowed = allowed & (key_pos[None, :] >= 0) & (query_seg[:, None] == key_seg[None, :])
        attention_logits = jnp.einsum("eqco,fqo->qcef", block_queries, block_keys) * logit_scale
        attention_logits = jnp.where(allowed, attention_logits, -1e30)
        top_score = jnp.max(attention_logits, axis=3, keepdims=True)
        weights = jnp.where(allowed, jnp.exp(attention_logits - top_score), 0.0)
        probs = weights / jnp.sum(weights, axis=3, keepdims=True)
        return probs, block_queries, block_keys, block_values, first_row

    def forward_block(block_index):
        probs, block_queries, block_keys, block_values, first_row = block_probs(block_index)
        rounded_values = probs.astype(jnp.bfloat16).astype(jnp.float32)
        attended_output = jnp.einsum("ykip,pyj->iykj", rounded_values, block_values)
        return attended_output.astype(jnp.bfloat16).reshape(rows_per_block, HQ * HEAD_WIDTH)

    attended_output = lax.map(forward_block, jnp.arange(block_count, dtype=jnp.int32)).reshape(SLAB_TOKENS, HQ * HEAD_WIDTH)
    layer_out = jnp.dot(attended_output, out_proj.T, preferred_element_type=jnp.float32).astype(jnp.bfloat16)
    grad_attended = jnp.dot(out_grad, out_proj, preferred_element_type=jnp.float32).astype(jnp.bfloat16)
    grad_proj = jnp.dot(out_grad.T, attended_output, preferred_element_type=jnp.float32) * (SLAB_TOKENS ** -0.5)

    def backward_block(carry, block_index):
        key_sum, value_sum = carry
        probs, block_queries, block_keys, block_values, first_row = block_probs(block_index)
        rounded_values = probs.astype(jnp.bfloat16).astype(jnp.float32)
        block_gradient = lax.dynamic_slice_in_dim(grad_attended, first_row, rows_per_block, 0).astype(jnp.float32)
        block_gradient = block_gradient.reshape(rows_per_block, KEY_VALUE_HEADS, QUERIES_PER_KV, HEAD_WIDTH)
        attention_block = lax.dynamic_slice_in_dim(attended_output, first_row, rows_per_block, 0).astype(jnp.float32)
        attention_block = attention_block.reshape(rows_per_block, KEY_VALUE_HEADS, QUERIES_PER_KV, HEAD_WIDTH)
        probability_gradient = jnp.einsum("eqco,fqo->qcef", block_gradient, block_values)
        row_delta = jnp.transpose(jnp.sum(block_gradient * attention_block, axis=3), (1, 2, 0))[..., None]
        score_gradient = (probs * (probability_gradient - row_delta)).astype(jnp.bfloat16).astype(jnp.float32)
        query_gradient = logit_scale * jnp.einsum("ykip,pyj->iykj", score_gradient, block_keys)
        query_gradient = query_gradient.astype(jnp.bfloat16).reshape(rows_per_block, HQ, HEAD_WIDTH)
        key_portion = logit_scale * jnp.einsum("huoe,ohul->ehl", score_gradient, block_queries)
        value_portion = jnp.einsum("huoe,ohul->ehl", rounded_values, block_gradient)
        key_sum = lax.dynamic_update_slice_in_dim(
            key_sum, lax.dynamic_slice_in_dim(key_sum, first_row, span_rows, 0) + key_portion, first_row, 0)
        value_sum = lax.dynamic_update_slice_in_dim(
            value_sum, lax.dynamic_slice_in_dim(value_sum, first_row, span_rows, 0) + value_portion, first_row, 0)
        return (key_sum, value_sum), query_gradient

    zero_sum_rows = jnp.zeros((SLAB_TOKENS + WINDOW_TOKENS, KEY_VALUE_HEADS, HEAD_WIDTH), jnp.float32)
    (key_sum, value_sum), query_gradient = lax.scan(
        backward_block, (zero_sum_rows, zero_sum_rows), jnp.arange(block_count, dtype=jnp.int32))
    query_gradient = query_gradient.reshape(SLAB_TOKENS, HQ, HEAD_WIDTH)
    grad_key = key_sum[WINDOW_TOKENS:].astype(jnp.bfloat16)
    grad_value = value_sum[WINDOW_TOKENS:].astype(jnp.bfloat16)
    return (layer_out, query_gradient, grad_key, grad_value, grad_proj)
```

```python
import jax
import jax.numpy as jnp
from jax import lax
from jax.sharding import PartitionSpec as P

WINDOW_TOKENS = 1024


def passed_along(value, axis, by):
    count = lax.axis_size(axis)
    pairs = [(i, i + by) for i in range(count) if 0 <= i + by < count]
    return lax.ppermute(value, axis, pairs)


def shards(queries, rotated_keys, value_vectors, out_grad, out_proj, seg_ids):
    logit_scale = 168.0 ** (-0.5)
    tok_rows = queries.shape[0]
    heads_query = queries.shape[1]
    heads_kv = rotated_keys.shape[1]
    head_size = queries.shape[2]
    group_size = heads_query // heads_kv
    blocks = WINDOW_TOKENS // tok_rows
    ctx_count = lax.axis_size("ctx")
    ctx_index = lax.axis_index("ctx")
    own_block = jnp.stack([rotated_keys, value_vectors])
    received = []
    for offset in range(blocks):
        received.append(passed_along(own_block, "ctx", offset + 1))
    key_value = jnp.concatenate(received[::-1] + [own_block], axis=1)
    key_row_slice = key_value[0]
    value_row_slice = key_value[1]
    first_row = ctx_index * tok_rows
    seg_padded = jnp.concatenate([jnp.full((WINDOW_TOKENS,), -1, jnp.int32), seg_ids], 0)
    key_seg = lax.dynamic_slice_in_dim(seg_padded, first_row, WINDOW_TOKENS + tok_rows, 0)
    query_seg = lax.dynamic_slice_in_dim(seg_ids, first_row, tok_rows, 0)
    query_pos = first_row + jnp.arange(tok_rows, dtype=jnp.int32)
    key_pos = first_row - WINDOW_TOKENS + jnp.arange(WINDOW_TOKENS + tok_rows, dtype=jnp.int32)
    allowed = (key_pos[None, :] <= query_pos[:, None]) & (
        query_pos[:, None] - key_pos[None, :] < WINDOW_TOKENS
    )
    allowed = allowed & (key_pos[None, :] >= 0) & (query_seg[:, None] == key_seg[None, :])
    grouped_queries = queries.reshape(tok_rows, heads_kv, group_size, head_size)
    attention_logits = logit_scale * jnp.einsum(
        "eqco,fqo->qcef", grouped_queries, key_row_slice, preferred_element_type=jnp.float32
    )
    attention_logits = jnp.where(allowed, attention_logits, -1e30)
    top_score = jnp.max(attention_logits, axis=3, keepdims=True)
    weights = jnp.where(allowed, jnp.exp(attention_logits - top_score), 0.0)
    probs = weights / jnp.sum(weights, axis=3, keepdims=True)
    probabilities_half = probs.astype(jnp.bfloat16)
    attended_output = jnp.einsum(
        "ykip,pyj->iykj", probabilities_half, value_row_slice, preferred_element_type=jnp.float32
    )
    attended_output = attended_output.astype(jnp.bfloat16).reshape(
        tok_rows, heads_query * head_size
    )
    proj_full = lax.all_gather(out_proj, "ctx", axis=0, tiled=True)
    out_partial = lax.dot_general(
        attended_output, proj_full, (((1,), (1,)), ((), ())), preferred_element_type=jnp.float32
    )
    layer_out = lax.psum_scatter(out_partial, "head", scatter_dimension=1, tiled=True).astype(
        jnp.bfloat16
    )
    grad_full = lax.all_gather(out_grad, "head", axis=1, tiled=True)
    grad_attended = jnp.dot(grad_full, proj_full, preferred_element_type=jnp.float32).astype(
        jnp.bfloat16
    )
    proj_rows = grad_full.shape[1] // ctx_count
    proj_partial = jnp.einsum(
        "tcr,tj->crj",
        grad_full.reshape(tok_rows, ctx_count, proj_rows),
        attended_output,
        preferred_element_type=jnp.float32,
    )
    proj_summed = lax.psum_scatter(proj_partial, "ctx", scatter_dimension=0, tiled=True)
    grad_proj = proj_summed.reshape(proj_rows, -1) * (ctx_count * tok_rows) ** (-0.5)
    grouped_gradient = grad_attended.reshape(tok_rows, heads_kv, group_size, head_size)
    attn_groups = attended_output.reshape(tok_rows, heads_kv, group_size, head_size)
    probability_gradient = jnp.einsum(
        "eqco,fqo->qcef", grouped_gradient, value_row_slice, preferred_element_type=jnp.float32
    )
    row_delta = jnp.sum(
        grouped_gradient.astype(jnp.float32) * attn_groups.astype(jnp.float32), axis=3
    )
    row_delta = jnp.transpose(row_delta, (1, 2, 0))[..., None]
    score_gradient = (probs * (probability_gradient - row_delta)).astype(jnp.bfloat16)
    query_gradient = logit_scale * jnp.einsum(
        "ykip,pyj->iykj", score_gradient, key_row_slice, preferred_element_type=jnp.float32
    )
    query_gradient = query_gradient.astype(jnp.bfloat16).reshape(tok_rows, heads_query, head_size)
    key_portion = logit_scale * jnp.einsum(
        "huoe,ohul->ehl", score_gradient, grouped_queries, preferred_element_type=jnp.float32
    )
    value_portion = jnp.einsum(
        "huoe,ohul->ehl", probabilities_half, grouped_gradient, preferred_element_type=jnp.float32
    )
    both_parts = jnp.stack([key_portion, value_portion])
    halo_part = both_parts[:, :WINDOW_TOKENS]
    summed = both_parts[:, WINDOW_TOKENS:]
    for offset in range(blocks):
        distance = offset + 1
        portion = halo_part[:, (blocks - distance) * tok_rows : (blocks - distance + 1) * tok_rows]
        summed = summed + passed_along(portion, "ctx", -distance)
    grad_key = summed[0].astype(jnp.bfloat16)
    grad_value = summed[1].astype(jnp.bfloat16)
    return (layer_out, query_gradient, grad_key, grad_value, grad_proj)


def solution(mesh):
    return jax.shard_map(
        shards,
        mesh=mesh,
        in_specs=(
            P("ctx", "head", None),
            P("ctx", "head", None),
            P("ctx", "head", None),
            P("ctx", "head"),
            P("ctx", "head"),
            P(),
        ),
        out_specs=(
            P("ctx", "head"),
            P("ctx", "head", None),
            P("ctx", "head", None),
            P("ctx", "head", None),
            P("ctx", "head"),
        ),
        check_vma=False,
    )
```

```python
import jax
import jax.numpy as jnp
from jax import lax
from jax.sharding import PartitionSpec as P

WINDOW_TOKENS = 1024


def passed_along(value, axis, by):
    count = lax.axis_size(axis)
    pairs = [(i, i + by) for i in range(count) if 0 <= i + by < count]
    return lax.ppermute(value, axis, pairs)


def shards(queries, rotated_keys, value_vectors, out_grad, out_proj, seg_ids):
    logit_scale = 168.0 ** (-0.5)
    tok_rows = queries.shape[0]
    heads_query = queries.shape[1]
    heads_kv = rotated_keys.shape[1]
    head_size = queries.shape[2]
    group_size = heads_query // heads_kv
    blocks = WINDOW_TOKENS // tok_rows
    ctx_count = lax.axis_size("ctx")
    ctx_index = lax.axis_index("ctx")
    own_block = jnp.stack([rotated_keys, value_vectors])
    received = []
    for offset in range(blocks):
        received.append(passed_along(own_block, "ctx", offset + 1))
    key_value = jnp.concatenate(received[::-1] + [own_block], axis=1)
    key_row_slice = key_value[0]
    value_row_slice = key_value[1]
    first_row = ctx_index * tok_rows
    seg_padded = jnp.concatenate([jnp.full((WINDOW_TOKENS,), -1, jnp.int32), seg_ids], 0)
    key_seg = lax.dynamic_slice_in_dim(seg_padded, first_row, WINDOW_TOKENS + tok_rows, 0)
    query_seg = lax.dynamic_slice_in_dim(seg_ids, first_row, tok_rows, 0)
    query_pos = first_row + jnp.arange(tok_rows, dtype=jnp.int32)
    key_pos = first_row - WINDOW_TOKENS + jnp.arange(WINDOW_TOKENS + tok_rows, dtype=jnp.int32)
    allowed = (key_pos[None, :] <= query_pos[:, None]) & (
        query_pos[:, None] - key_pos[None, :] < WINDOW_TOKENS
    )
    allowed = allowed & (key_pos[None, :] >= 0) & (query_seg[:, None] == key_seg[None, :])
    grouped_queries = queries.reshape(tok_rows, heads_kv, group_size, head_size)
    attention_logits = logit_scale * jnp.einsum(
        "eqco,fqo->qcef", grouped_queries, key_row_slice, preferred_element_type=jnp.float32
    )
    attention_logits = jnp.where(allowed, attention_logits, -1e30)
    top_score = jnp.max(attention_logits, axis=3, keepdims=True)
    weights = jnp.where(allowed, jnp.exp(attention_logits - top_score), 0.0)
    probs = weights / jnp.sum(weights, axis=3, keepdims=True)
    probabilities_half = probs.astype(jnp.bfloat16)
    attended_output = jnp.einsum(
        "ykip,pyj->iykj", probabilities_half, value_row_slice, preferred_element_type=jnp.float32
    )
    attended_output = attended_output.astype(jnp.bfloat16).reshape(
        tok_rows, heads_query * head_size
    )
    proj_full = lax.all_gather(out_proj, "ctx", axis=0, tiled=True)
    out_partial = lax.dot_general(
        attended_output, proj_full, (((1,), (1,)), ((), ())), preferred_element_type=jnp.float32
    )
    layer_out = lax.psum_scatter(out_partial, "head", scatter_dimension=1, tiled=True).astype(
        jnp.bfloat16
    )
    grad_full = lax.all_gather(out_grad, "head", axis=1, tiled=True)
    grad_attended = jnp.dot(grad_full, proj_full, preferred_element_type=jnp.float32).astype(
        jnp.bfloat16
    )
    proj_rows = grad_full.shape[1] // ctx_count
    proj_partial = jnp.einsum(
        "tcr,tj->crj",
        grad_full.reshape(tok_rows, ctx_count, proj_rows),
        attended_output,
        preferred_element_type=jnp.float32,
    )
    proj_pieces = lax.all_to_all(
        proj_partial.astype(jnp.bfloat16), "ctx", split_axis=0, concat_axis=0, tiled=True
    )
    proj_summed = jnp.sum(proj_pieces.astype(jnp.float32), axis=0)
    grad_proj = proj_summed * (ctx_count * tok_rows) ** (-0.5)
    grouped_gradient = grad_attended.reshape(tok_rows, heads_kv, group_size, head_size)
    attn_groups = attended_output.reshape(tok_rows, heads_kv, group_size, head_size)
    probability_gradient = jnp.einsum(
        "eqco,fqo->qcef", grouped_gradient, value_row_slice, preferred_element_type=jnp.float32
    )
    row_delta = jnp.sum(
        grouped_gradient.astype(jnp.float32) * attn_groups.astype(jnp.float32), axis=3
    )
    row_delta = jnp.transpose(row_delta, (1, 2, 0))[..., None]
    score_gradient = (probs * (probability_gradient - row_delta)).astype(jnp.bfloat16)
    query_gradient = logit_scale * jnp.einsum(
        "ykip,pyj->iykj", score_gradient, key_row_slice, preferred_element_type=jnp.float32
    )
    query_gradient = query_gradient.astype(jnp.bfloat16).reshape(tok_rows, heads_query, head_size)
    key_portion = logit_scale * jnp.einsum(
        "huoe,ohul->ehl", score_gradient, grouped_queries, preferred_element_type=jnp.float32
    )
    value_portion = jnp.einsum(
        "huoe,ohul->ehl", probabilities_half, grouped_gradient, preferred_element_type=jnp.float32
    )
    both_parts = jnp.stack([key_portion, value_portion])
    halo_part = both_parts[:, :WINDOW_TOKENS]
    summed = both_parts[:, WINDOW_TOKENS:]
    for offset in range(blocks):
        distance = offset + 1
        portion = halo_part[:, (blocks - distance) * tok_rows : (blocks - distance + 1) * tok_rows]
        summed = summed + passed_along(portion, "ctx", -distance)
    grad_key = summed[0].astype(jnp.bfloat16)
    grad_value = summed[1].astype(jnp.bfloat16)
    return (layer_out, query_gradient, grad_key, grad_value, grad_proj)


def solution(mesh):
    return jax.shard_map(
        shards,
        mesh=mesh,
        in_specs=(
            P("ctx", "head", None),
            P("ctx", "head", None),
            P("ctx", "head", None),
            P("ctx", "head"),
            P("ctx", "head"),
            P(),
        ),
        out_specs=(
            P("ctx", "head"),
            P("ctx", "head", None),
            P("ctx", "head", None),
            P("ctx", "head", None),
            P("ctx", "head"),
        ),
        check_vma=False,
    )
```

```python
import jax
import jax.numpy as jnp
from jax import lax
from jax.sharding import PartitionSpec as P

WINDOW_TOKENS = 1024


def passed_along(value, axis, by):
    count = lax.axis_size(axis)
    pairs = [(i, i + by) for i in range(count) if 0 <= i + by < count]
    return lax.ppermute(value, axis, pairs)


def shards(queries, rotated_keys, value_vectors, out_grad, out_proj, seg_ids):
    logit_scale = 168.0 ** (-0.5)
    tok_rows = queries.shape[0]
    heads_query = queries.shape[1]
    heads_kv = rotated_keys.shape[1]
    head_size = queries.shape[2]
    group_size = heads_query // heads_kv
    blocks = WINDOW_TOKENS // tok_rows
    ctx_count = lax.axis_size("ctx")
    ctx_index = lax.axis_index("ctx")
    own_block = jnp.stack([rotated_keys, value_vectors])
    received = []
    for offset in range(blocks):
        received.append(passed_along(own_block, "ctx", offset + 1))
    key_value = jnp.concatenate(received[::-1] + [own_block], axis=1)
    key_row_slice = key_value[0]
    value_row_slice = key_value[1]
    first_row = ctx_index * tok_rows
    seg_padded = jnp.concatenate([jnp.full((WINDOW_TOKENS,), -1, jnp.int32), seg_ids], 0)
    key_seg = lax.dynamic_slice_in_dim(seg_padded, first_row, WINDOW_TOKENS + tok_rows, 0)
    query_seg = lax.dynamic_slice_in_dim(seg_ids, first_row, tok_rows, 0)
    query_pos = first_row + jnp.arange(tok_rows, dtype=jnp.int32)
    key_pos = first_row - WINDOW_TOKENS + jnp.arange(WINDOW_TOKENS + tok_rows, dtype=jnp.int32)
    allowed = (key_pos[None, :] <= query_pos[:, None]) & (
        query_pos[:, None] - key_pos[None, :] < WINDOW_TOKENS
    )
    allowed = allowed & (key_pos[None, :] >= 0) & (query_seg[:, None] == key_seg[None, :])
    grouped_queries = queries.reshape(tok_rows, heads_kv, group_size, head_size)
    attention_logits = logit_scale * jnp.einsum(
        "eqco,fqo->qcef", grouped_queries, key_row_slice, preferred_element_type=jnp.float32
    )
    attention_logits = jnp.where(allowed, attention_logits, -1e30)
    top_score = jnp.max(attention_logits, axis=3, keepdims=True)
    weights = jnp.where(allowed, jnp.exp(attention_logits - top_score), 0.0)
    probs = weights / jnp.sum(weights, axis=3, keepdims=True)
    probabilities_half = probs.astype(jnp.bfloat16)
    attended_output = jnp.einsum(
        "ykip,pyj->iykj", probabilities_half, value_row_slice, preferred_element_type=jnp.float32
    )
    attended_output = attended_output.astype(jnp.bfloat16).reshape(
        tok_rows, heads_query * head_size
    )
    grad_full = lax.all_gather(out_grad, "head", axis=1, tiled=True)
    proj_rows = grad_full.shape[1] // ctx_count
    proj_partial = jnp.einsum(
        "tcr,tj->crj",
        grad_full.reshape(tok_rows, ctx_count, proj_rows),
        attended_output,
        preferred_element_type=jnp.float32,
    ).astype(jnp.bfloat16)
    proj_partial, out_proj = lax.optimization_barrier((proj_partial, out_proj))
    proj_pieces = lax.all_to_all(proj_partial, "ctx", split_axis=0, concat_axis=0, tiled=True)
    proj_full = lax.all_gather(out_proj, "ctx", axis=0, tiled=True)
    out_partial = lax.dot_general(
        attended_output, proj_full, (((1,), (1,)), ((), ())), preferred_element_type=jnp.float32
    )
    layer_out = lax.psum_scatter(out_partial, "head", scatter_dimension=1, tiled=True).astype(
        jnp.bfloat16
    )
    grad_attended = jnp.dot(grad_full, proj_full, preferred_element_type=jnp.float32).astype(
        jnp.bfloat16
    )
    proj_summed = jnp.sum(proj_pieces.astype(jnp.float32), axis=0)
    grad_proj = proj_summed * (ctx_count * tok_rows) ** (-0.5)
    grouped_gradient = grad_attended.reshape(tok_rows, heads_kv, group_size, head_size)
    attn_groups = attended_output.reshape(tok_rows, heads_kv, group_size, head_size)
    probability_gradient = jnp.einsum(
        "eqco,fqo->qcef", grouped_gradient, value_row_slice, preferred_element_type=jnp.float32
    )
    row_delta = jnp.sum(
        grouped_gradient.astype(jnp.float32) * attn_groups.astype(jnp.float32), axis=3
    )
    row_delta = jnp.transpose(row_delta, (1, 2, 0))[..., None]
    score_gradient = (probs * (probability_gradient - row_delta)).astype(jnp.bfloat16)
    query_gradient = logit_scale * jnp.einsum(
        "ykip,pyj->iykj", score_gradient, key_row_slice, preferred_element_type=jnp.float32
    )
    query_gradient = query_gradient.astype(jnp.bfloat16).reshape(tok_rows, heads_query, head_size)
    key_portion = logit_scale * jnp.einsum(
        "huoe,ohul->ehl", score_gradient, grouped_queries, preferred_element_type=jnp.float32
    )
    value_portion = jnp.einsum(
        "huoe,ohul->ehl", probabilities_half, grouped_gradient, preferred_element_type=jnp.float32
    )
    both_parts = jnp.stack([key_portion, value_portion])
    halo_part = both_parts[:, :WINDOW_TOKENS]
    summed = both_parts[:, WINDOW_TOKENS:]
    for offset in range(blocks):
        distance = offset + 1
        portion = halo_part[:, (blocks - distance) * tok_rows : (blocks - distance + 1) * tok_rows]
        summed = summed + passed_along(portion.astype(jnp.bfloat16), "ctx", -distance).astype(
            jnp.float32
        )
    grad_key = summed[0].astype(jnp.bfloat16)
    grad_value = summed[1].astype(jnp.bfloat16)
    return (layer_out, query_gradient, grad_key, grad_value, grad_proj)


def solution(mesh):
    return jax.shard_map(
        shards,
        mesh=mesh,
        in_specs=(
            P("ctx", "head", None),
            P("ctx", "head", None),
            P("ctx", "head", None),
            P("ctx", "head"),
            P("ctx", "head"),
            P(),
        ),
        out_specs=(
            P("ctx", "head"),
            P("ctx", "head", None),
            P("ctx", "head", None),
            P("ctx", "head", None),
            P("ctx", "head"),
        ),
        check_vma=False,
    )
```
